1024 devices in a mesh: ctx: 16 (over y, x), exp: 64 (over z, core).
Axes of the slice: x: 4, y: 4, z: 32, core: 2. Of those that a mesh axis runs over, the one named last changes fastest.
Arguments:
- queries: bfloat16 [64, 2048, 1536], P('exp', 'ctx'), may hold values from -6 to 6
- keys: bfloat16 [64, 2048, 1536], P('exp', 'ctx'), may hold values from -6 to 6
- values: bfloat16 [64, 2048, 1536], P('exp', 'ctx'), may hold values from -6 to 6
- log_decay: float32 [24, 64, 2048], P(None, 'exp', 'ctx'), may hold values from -0.9 to 0
- resid: bfloat16 [64, 2048, 1536], P('exp', 'ctx'), may hold values from -4 to 4
- gate_in: bfloat16 [64, 2048, 1536], P('exp', 'ctx'), may hold values from -8 to 8
- attn_gain: float32 [1536], replicated, may hold values from 0.5 to 1.5
- moe_gain: float32 [1536], replicated, may hold values from 0.5 to 1.5
- router_weight: bfloat16 [1536, 64], replicated, may hold values from -0.091796875 to 0.091796875
- expert_ids: int32 [64, 2048, 2], P('exp', 'ctx'), may hold values from 0 to 63, all different within a row; in each aligned block of 128 rows (0 to 127, 128 to 255, ..., all dimensions but the last counted through in order) at most 8 rows name the same one
- gate_weight: bfloat16 [64, 1536, 512], P('exp'), may hold values from -0.15625 to 0.15625
- up_weight: bfloat16 [64, 1536, 512], P('exp'), may hold values from -0.15625 to 0.15625
- down_weight: bfloat16 [64, 512, 1536], P('exp'), may hold values from -0.5 to 0.5
Outputs:
- layer_out: bfloat16 [64, 2048, 1536], P('exp', 'ctx')
The draws below stay inside these ranges and needn't reach their ends.
Inputs may be any that keep to these rules, and one draw needn't show every extreme that they name: `expert_ids`: each token names 2 different experts. Among the 128 positions of one block of one document no expert is named more than 8 times, and in some blocks one is named exactly 8 times.
All inputs are finite; a program needn't handle non-finite values.
Results may differ from the reference program's by a relative error of at most 0.013.
Values may be sent and summed in bfloat16 or wider, within the bound.
No kernel may reach another device: no remote copies, remote signals or barrier semaphores. Data moves between devices by JAX's collectives and lax.ppermute only.
A program may use at most 64 MiB of HBM per device.

```python
import math
import jax
import jax.numpy as jnp
import numpy as np
from jax import lax

HEADS = 24
HD = 64
D = 1536
FF = 512
EXPERTS = 64
TOP = 2
TOK_DEV = 128
CAP = 8
DOCUMENT_COUNT = 64
DOCUMENT_LENGTH = 2048
N_CTX = 16


def draw_log_decay(key, part):
    random_split_keys = jax.random.split(key, 7)
    slow_share = 0.5
    is_slow = jax.random.bernoulli(random_split_keys[0], slow_share, (HEADS, DOCUMENT_COUNT, 1))
    slow_rate = jnp.exp(jax.random.uniform(random_split_keys[1], (HEADS, DOCUMENT_COUNT, 1), jnp.float32, jnp.log(0.03), jnp.log(0.25))) / DOCUMENT_LENGTH
    fast_rate = jnp.exp(jax.random.uniform(random_split_keys[2], (HEADS, DOCUMENT_COUNT, 1), jnp.float32, jnp.log(1.0 / 50.0), jnp.log(1.0 / 30.0)))
    baseline_decay_rate = jnp.where(is_slow, slow_rate, fast_rate)
    per_block_scale = jnp.repeat(jax.random.uniform(random_split_keys[3], (HEADS, DOCUMENT_COUNT, DOCUMENT_LENGTH // TOK_DEV), jnp.float32, 0.6, 1.5), TOK_DEV, axis=2)
    per_token_scale = jax.random.uniform(random_split_keys[4], (HEADS, DOCUMENT_COUNT, DOCUMENT_LENGTH), jnp.float32, 0.5, 1.5)
    sudden_spike = jax.random.bernoulli(random_split_keys[5], 3.0 / DOCUMENT_LENGTH, (1, DOCUMENT_COUNT, DOCUMENT_LENGTH))
    logged_decay_drop = jnp.log(jax.random.uniform(random_split_keys[6], (1, DOCUMENT_COUNT, DOCUMENT_LENGTH), jnp.float32, 0.45, 0.8))
    return -baseline_decay_rate * per_block_scale * per_token_scale + jnp.where(sudden_spike, logged_decay_drop, 0.0)


def steps_of(key, extent, cuts, least, top_value):
    def one(axis_at, blocks):
        heights = jax.random.uniform(jax.random.fold_in(jax.random.fold_in(key, 6), axis_at), (blocks,), jnp.float32, least / len(cuts), top_value / len(cuts))
        return jnp.repeat(jnp.exp(heights), extent[axis_at] // blocks).reshape((-1,) + (1,) * (len(extent) - axis_at - 1))

    factor_of = one(*cuts[0])
    for cut in cuts[1:]:
        factor_of = factor_of * one(*cut)
    return factor_of


def shared_out(stream_key, own, number, rows, count, top, bound, skew):
    sequence = jax.random.permutation(stream_key, count)
    heavy_load, ordinary = load_shares(count, rows * top, bound, skew, True), load_shares(count, rows * top, bound, skew, False)
    places = jnp.arange(count)

    def named(tallies, offset_by):
        used = int((tallies > 0).sum())
        fixed = max(1, used // 4)
        moved = fixed + (places - fixed + offset_by * (used - fixed)) % max(1, count - fixed)
        return jnp.zeros((count,), jnp.int32).at[sequence[jnp.where(places < fixed, places, moved)]].set(jnp.asarray(tallies, jnp.int32))

    tallies = jnp.where(number % 4 == 0, named(heavy_load, number // 4), named(ordinary, number - number // 4 - 1))
    mixed = jax.random.permutation(jax.random.fold_in(own, 3), count)
    giver, sink = mixed[0:count // 2 * 2:2], mixed[1:count // 2 * 2:2]
    slack = jnp.minimum(tallies[giver] - 1, bound - tallies[sink]) // 2
    slack = jnp.where((giver == sequence[0]) | (sink == sequence[0]) | (tallies[sink] == 0), 0, jnp.maximum(slack, 0))
    moved = jax.random.randint(jax.random.fold_in(own, 4), (count // 2,), 0, 1 << 20) % (slack + 1)
    tallies = tallies.at[giver].add(-moved).at[sink].add(moved)
    members = jnp.searchsorted(jnp.cumsum(tallies), jnp.arange(rows * top), side="right").astype(jnp.int32)
    table = members.reshape(top, rows).T
    table = table[jax.random.permutation(jax.random.fold_in(own, 1), rows)]
    offset_by = jax.random.randint(jax.random.fold_in(own, 2), (rows, 1), 0, top)
    return jnp.take_along_axis(table, (jnp.arange(top)[None, :] + offset_by) % top, axis=1)


def load_shares(count, total, bound, lean, full):
    weights = [(1 << 20) // math.isqrt(standing ** lean) + 1 for standing in range(1, count + 1)]
    largest = bound if full else min(bound, max(-(-total // count), total * weights[0] // sum(weights)))
    least = 1 if total - largest >= count - 1 else 0
    given, surplus = [largest] + [least] * (count - 1), total - largest - least * (count - 1)
    while surplus > 0:
        free = [i for i in range(1, count) if given[i] < largest] or [i for i in range(1, count) if given[i] < bound]
        pool, left = sum([weights[i] for i in free]), surplus
        for i in free:
            extra = min(bound - given[i], max(1, left * weights[i] // pool), surplus)
            given[i] = given[i] + extra
            surplus = surplus - extra
    return np.array(given)


def scatter_about(stream_key, shape, width, reach, cuts=(), kind=jnp.bfloat16):
    entries = width * jax.random.normal(stream_key, shape, jnp.float32)
    if cuts:
        entries = entries * steps_of(stream_key, shape, cuts, -0.22, 0.18)
    return jnp.clip(entries, -reach, reach).astype(kind)


def setup_inputs(seed: int = 0) -> dict:
    streams_of = jax.random.split(jax.random.key(seed), 14)
    queries = scatter_about(streams_of[0], (DOCUMENT_COUNT, DOCUMENT_LENGTH, D), 1.0, 6.0, ((0, 64), (1, 16)))
    keys = scatter_about(streams_of[1], (DOCUMENT_COUNT, DOCUMENT_LENGTH, D), 1.0, 6.0, ((0, 64), (1, 16)))
    values = scatter_about(streams_of[2], (DOCUMENT_COUNT, DOCUMENT_LENGTH, D), 1.0, 6.0, ((0, 64), (1, 16)))
    log_decay = draw_log_decay(jax.random.fold_in(streams_of[13], 71), 0)
    resid = scatter_about(streams_of[4], (DOCUMENT_COUNT, DOCUMENT_LENGTH, D), 0.5, 4.0, ((0, 64), (1, 16)))
    gate_in = scatter_about(streams_of[5], (DOCUMENT_COUNT, DOCUMENT_LENGTH, D), 1.5, 8.0, ((0, 64), (1, 16)))
    attn_gain = jnp.clip(1.0 + 0.1 * jax.random.normal(streams_of[6], (D,), jnp.float32), 0.5, 1.5)
    moe_gain = jnp.clip(1.0 + 0.1 * jax.random.normal(streams_of[7], (D,), jnp.float32), 0.5, 1.5)
    router_weight = scatter_about(streams_of[8], (D, EXPERTS), (0.6 / D ** 0.5), 0.091796875)
    expert_ids_keys = jax.random.split(jax.random.fold_in(streams_of[9], 1), DOCUMENT_COUNT * DOCUMENT_LENGTH // TOK_DEV)
    expert_ids_turns = jax.random.permutation(jax.random.fold_in(streams_of[9], 3), DOCUMENT_COUNT * DOCUMENT_LENGTH // TOK_DEV)
    expert_ids = jax.vmap(lambda own, number: shared_out(jax.random.fold_in(streams_of[9], 2), own, number, TOK_DEV, EXPERTS, TOP, CAP, 2))(expert_ids_keys, expert_ids_turns).reshape((DOCUMENT_COUNT, DOCUMENT_LENGTH, TOP))
    gate_weight = scatter_about(streams_of[10], (EXPERTS, D, FF), D ** -0.5, 0.15625, ((0, 64),))
    up_weight = scatter_about(streams_of[11], (EXPERTS, D, FF), D ** -0.5, 0.15625, ((0, 64),))
    down_weight = scatter_about(streams_of[12], (EXPERTS, FF, D), (FF // 4) ** -0.5, 0.5, ((0, 64),))
    return {"queries": queries, "keys": keys, "values": values, "log_decay": log_decay, "resid": resid, "gate_in": gate_in, "attn_gain": attn_gain, "moe_gain": moe_gain, "router_weight": router_weight, "expert_ids": expert_ids, "gate_weight": gate_weight, "up_weight": up_weight, "down_weight": down_weight}


HIGHEST = lax.Precision.HIGHEST

def block_attention(q_rows, k_rows, v_rows, decay_log, entering):
    inv_root = q_rows.shape[-1] ** (-0.5)
    cumulated = jnp.cumsum(decay_log, axis=1)
    positions = jnp.arange(q_rows.shape[0], dtype=jnp.int32)
    causal = (positions[:, None] >= positions[None, :])[None]
    gap_log = jnp.where(causal, cumulated[:, :, None] - cumulated[:, None, :], 0.0)
    damping = jnp.where(causal, jnp.exp(gap_log), 0.0)
    scores = jnp.einsum('thd,shd->hts', q_rows.astype(jnp.float32), k_rows.astype(jnp.float32)) * inv_root * damping
    scores = lax.optimization_barrier(scores.astype(jnp.bfloat16))
    local_part = jnp.einsum('hts,shd->thd', scores.astype(jnp.float32), v_rows.astype(jnp.float32))
    carried = jnp.einsum('thd,hde->the', q_rows.astype(jnp.float32), entering, precision=HIGHEST) * (inv_root * jnp.exp(cumulated)).T[:, :, None]
    block_decay = jnp.exp(cumulated[:, -1])
    tail_decay = jnp.exp(cumulated[:, -1:] - cumulated)
    k_scaled = k_rows.astype(jnp.float32) * tail_decay.T[:, :, None]
    contribution = jnp.einsum('thd,the->hde', k_scaled, v_rows.astype(jnp.float32), precision=HIGHEST)
    return (local_part + carried, block_decay, contribution)

def document(pieces):
    q_doc, k_doc, v_doc, decay_doc = pieces
    q_blocks = q_doc.reshape(N_CTX, TOK_DEV, HEADS, HD)
    k_blocks = k_doc.reshape(N_CTX, TOK_DEV, HEADS, HD)
    v_blocks = v_doc.reshape(N_CTX, TOK_DEV, HEADS, HD)
    decay_blocks = decay_doc.reshape(HEADS, N_CTX, TOK_DEV).transpose(1, 0, 2)

    def advance(entering, block_in):
        attended, block_decay, contribution = block_attention(block_in[0], block_in[1], block_in[2], block_in[3], entering)
        return (block_decay[:, None, None] * entering + contribution, attended)
    start_state = jnp.zeros((HEADS, HD, HD), jnp.float32)
    _, attended = lax.scan(advance, start_state, (q_blocks, k_blocks, v_blocks, decay_blocks))
    return attended.reshape(DOCUMENT_LENGTH, HEADS, HD)

def attend_out(attention, resid, gate_in, attn_gain):
    mean_square = lax.optimization_barrier(jnp.mean(attention * attention, axis=-1, keepdims=True))
    normalized = (attention * lax.rsqrt(mean_square + 1e-05)).reshape(resid.shape) * attn_gain
    return (resid.astype(jnp.float32) + normalized * jax.nn.sigmoid(gate_in.astype(jnp.float32))).astype(jnp.bfloat16)

def moe_input(hidden, moe_gain):
    h_float = lax.optimization_barrier(hidden).astype(jnp.float32)
    mean_square = lax.optimization_barrier(jnp.mean(h_float * h_float, axis=-1, keepdims=True))
    return (h_float * lax.rsqrt(mean_square + 1e-06) * moe_gain).astype(jnp.bfloat16)

def gate_share(normed, router_weight, chosen):
    affinity = jax.nn.sigmoid(jnp.dot(normed, router_weight, preferred_element_type=jnp.float32))
    labels = jnp.arange(router_weight.shape[1], dtype=jnp.int32)
    picks = (chosen[:, :, None] == labels[None, None, :]).astype(jnp.float32)
    picked = lax.optimization_barrier(jnp.sum(picks * affinity[:, None, :], axis=2))
    return picked / lax.optimization_barrier(jnp.sum(picked, axis=1, keepdims=True))

def reference(queries, keys, values, log_decay, resid, gate_in, attn_gain, moe_gain, router_weight, expert_ids, gate_weight, up_weight, down_weight):
    attention = lax.map(document, (queries, keys, values, jnp.transpose(log_decay, (1, 0, 2))))
    hidden = attend_out(attention, resid, gate_in, attn_gain)
    all_tokens = DOCUMENT_COUNT * DOCUMENT_LENGTH
    flat_rows = hidden.reshape(all_tokens, D)
    normed = moe_input(flat_rows, moe_gain)
    chosen = expert_ids.reshape(all_tokens, TOP)
    shares = gate_share(normed, router_weight, chosen)
    blocks = DOCUMENT_COUNT * N_CTX
    per_block = chosen.reshape(blocks, TOK_DEV * TOP)
    onehot = (per_block[:, :, None] == jnp.arange(EXPERTS, dtype=jnp.int32)[None, None, :]).astype(jnp.int32)
    before = jnp.cumsum(onehot, axis=1) - onehot
    slot_rank = lax.optimization_barrier(jnp.sum(before * onehot, axis=2))
    column = (jnp.arange(blocks, dtype=jnp.int32)[:, None] * CAP + slot_rank).reshape(-1).astype(jnp.int32)
    token_index = (jnp.arange(all_tokens * TOP, dtype=jnp.int32) // TOP).astype(jnp.int32)
    expert_col = chosen.reshape(-1).astype(jnp.int32)
    row_table = jnp.full((EXPERTS, blocks * CAP), all_tokens, jnp.int32).at[expert_col, column].set(token_index)
    share_table = jnp.zeros((EXPERTS, blocks * CAP), jnp.float32).at[expert_col, column].set(shares.reshape(-1))
    padded = jnp.concatenate([normed, jnp.zeros((1, D), normed.dtype)], axis=0)

    def serve_expert(accumulated, pieces):
        w_gate, w_up, w_down, row_index, share_col = pieces
        gathered = padded[row_index]
        gate_act = jnp.dot(gathered, w_gate, preferred_element_type=jnp.float32)
        up_act = jnp.dot(gathered, w_up, preferred_element_type=jnp.float32)
        inner_act = (jax.nn.silu(gate_act) * up_act).astype(jnp.bfloat16)
        result = jnp.dot(inner_act, w_down, preferred_element_type=jnp.float32).astype(jnp.bfloat16)
        result = lax.optimization_barrier(result).astype(jnp.float32)
        return (accumulated.at[row_index].add(share_col[:, None] * result), None)
    start_sum = jnp.zeros((all_tokens + 1, D), jnp.float32)
    accumulated, _ = lax.scan(serve_expert, start_sum, (gate_weight, up_weight, down_weight, row_table, share_table))
    h_float = lax.optimization_barrier(flat_rows).astype(jnp.float32)
    return (h_float + accumulated[:all_tokens]).reshape(DOCUMENT_COUNT, DOCUMENT_LENGTH, D).astype(jnp.bfloat16)
```

```python
import jax
import jax.numpy as jnp
from jax import lax
from jax.sharding import PartitionSpec as P

HIGHEST = lax.Precision.HIGHEST


def entering_scan(block_decay, contribution, axis):
    count, mine = (lax.axis_size(axis), lax.axis_index(axis))
    shift_pairs = [(i, i + 1) for i in range(count - 1)]
    decay = lax.ppermute(block_decay, axis, shift_pairs)
    state = lax.ppermute(contribution, axis, shift_pairs)
    decay = jnp.where(mine == 0, jnp.ones_like(decay), decay)
    step = 1
    while step < count - 1:
        pairs = [(i, i + step) for i in range(count - step)]
        got_decay = lax.ppermute(decay, axis, pairs)
        got_state = lax.ppermute(state, axis, pairs)
        has = mine >= step
        state = jnp.where(has, decay[:, None, None] * got_state + state, state)
        decay = jnp.where(has, got_decay * decay, decay)
        step *= 2
    return state


def combine_state(earlier, later):
    return (earlier[0] * later[0], later[0][:, None, None] * earlier[1] + later[1])


def apply_experts(arrived, gate_weight, up_weight, down_weight):
    exp_dev = gate_weight.shape[0]
    item_count = arrived.shape[1]
    features = arrived.shape[2]
    grouped = arrived.reshape(-1, exp_dev, item_count, features)
    gate_act = jnp.einsum(
        "send,edf->senf", grouped, gate_weight, preferred_element_type=jnp.float32
    )
    up_act = jnp.einsum("send,edf->senf", grouped, up_weight, preferred_element_type=jnp.float32)
    inner_act = (jax.nn.silu(gate_act) * up_act).astype(jnp.bfloat16)
    result = jnp.einsum(
        "senf,efd->send", inner_act, down_weight, preferred_element_type=jnp.float32
    )
    return result.astype(jnp.bfloat16).reshape(-1, item_count, features)


def on_device(
    queries,
    keys,
    values,
    log_decay,
    resid,
    gate_in,
    attn_gain,
    moe_gain,
    router_weight,
    expert_ids,
    gate_weight,
    up_weight,
    down_weight,
):
    tok_rows = queries.shape[1]
    features = queries.shape[2]
    head_count = log_decay.shape[0]
    head_size = features // head_count
    inv_root = head_size ** (-0.5)
    q_rows = queries.reshape(tok_rows, head_count, head_size)
    k_rows = keys.reshape(tok_rows, head_count, head_size)
    v_rows = values.reshape(tok_rows, head_count, head_size)
    decay_log = log_decay.reshape(head_count, tok_rows)
    cumulated = jnp.cumsum(decay_log, axis=1)
    positions = jnp.arange(tok_rows, dtype=jnp.int32)
    causal = (positions[:, None] >= positions[None, :])[None]
    gap_log = jnp.where(causal, cumulated[:, :, None] - cumulated[:, None, :], 0.0)
    damping = jnp.where(causal, jnp.exp(gap_log), 0.0)
    scores = (
        jnp.einsum("thd,shd->hts", q_rows, k_rows, preferred_element_type=jnp.float32)
        * inv_root
        * damping
    )
    scores = scores.astype(jnp.bfloat16)
    local_part = jnp.einsum("hts,shd->thd", scores, v_rows, preferred_element_type=jnp.float32)
    block_decay = jnp.exp(cumulated[:, -1])
    tail_decay = jnp.exp(cumulated[:, -1:] - cumulated)
    k_scaled = k_rows.astype(jnp.float32) * tail_decay.T[:, :, None]
    contribution = jnp.einsum(
        "thd,the->hde", k_scaled, v_rows.astype(jnp.float32), precision=HIGHEST
    )
    entering = entering_scan(block_decay, contribution, "ctx")
    carried = (
        jnp.einsum("thd,hde->the", q_rows.astype(jnp.float32), entering, precision=HIGHEST)
        * (inv_root * jnp.exp(cumulated)).T[:, :, None]
    )
    attention = local_part + carried
    mean_square = jnp.mean(attention * attention, axis=-1, keepdims=True)
    flat_resid = resid.reshape(tok_rows, features)
    normalized = (attention * lax.rsqrt(mean_square + 1e-05)).reshape(
        tok_rows, features
    ) * attn_gain
    flat_rows = (
        flat_resid.astype(jnp.float32)
        + normalized * jax.nn.sigmoid(gate_in.reshape(tok_rows, features).astype(jnp.float32))
    ).astype(jnp.bfloat16)
    h_float = flat_rows.astype(jnp.float32)
    moe_square = jnp.mean(h_float * h_float, axis=-1, keepdims=True)
    normed = (h_float * lax.rsqrt(moe_square + 1e-06) * moe_gain).astype(jnp.bfloat16)
    top_count = expert_ids.shape[2]
    chosen = expert_ids.reshape(tok_rows, top_count)
    experts = gate_weight.shape[0] * lax.axis_size("exp")
    capacity = 2 * top_count * tok_rows // experts
    affinity = jax.nn.sigmoid(jnp.dot(normed, router_weight, preferred_element_type=jnp.float32))
    labels = jnp.arange(experts, dtype=jnp.int32)
    picks = (chosen[:, :, None] == labels[None, None, :]).astype(jnp.float32)
    picked = jnp.sum(picks * affinity[:, None, :], axis=2)
    shares = picked / jnp.sum(picked, axis=1, keepdims=True)
    listed = chosen.reshape(-1)
    onehot = (listed[:, None] == labels[None, :]).astype(jnp.int32)
    before = jnp.cumsum(onehot, axis=0) - onehot
    slot_index = listed * capacity + jnp.sum(before * onehot, axis=1)
    slot_labels = jnp.arange(experts * capacity, dtype=jnp.int32)
    placing = jnp.sum(
        slot_labels[:, None, None] == slot_index.reshape(tok_rows, top_count)[None], axis=2
    ).astype(jnp.bfloat16)
    outgoing = (
        jnp.dot(placing, normed, preferred_element_type=jnp.float32)
        .astype(jnp.bfloat16)
        .reshape(experts, capacity, features)
    )
    arrived = lax.all_to_all(outgoing, "exp", split_axis=0, concat_axis=0, tiled=True)
    produced = apply_experts(arrived, gate_weight, up_weight, down_weight)
    returned = lax.all_to_all(produced, "exp", split_axis=0, concat_axis=0, tiled=True)
    gathered = jnp.take(returned.reshape(-1, features), slot_index, axis=0).reshape(
        tok_rows, top_count, features
    )
    mixture = jnp.sum(shares[:, :, None] * gathered.astype(jnp.float32), axis=1)
    return (h_float + mixture).astype(jnp.bfloat16).reshape(1, tok_rows, features)


def solution(mesh):
    placed = (
        P("exp", "ctx", None),
        P("exp", "ctx", None),
        P("exp", "ctx", None),
        P(None, "exp", "ctx"),
        P("exp", "ctx", None),
        P("exp", "ctx", None),
        P(),
        P(),
        P(),
        P("exp", "ctx", None),
        P("exp", None, None),
        P("exp", None, None),
        P("exp", None, None),
    )
    return jax.shard_map(
        on_device, mesh=mesh, in_specs=placed, out_specs=P("exp", "ctx", None), check_vma=False
    )
```

```python
import jax
import jax.numpy as jnp
from jax import lax
from jax.sharding import PartitionSpec as P

HIGHEST = lax.Precision.HIGHEST


def entering_scan(block_decay, contribution, axis):
    count, mine = (lax.axis_size(axis), lax.axis_index(axis))
    rows = contribution.shape[1]
    decay_row = jnp.broadcast_to(block_decay[:, None, None], contribution.shape[:1] + (1,) + contribution.shape[2:])
    packed = jnp.concatenate([contribution, decay_row], axis=1)

    def split(value):
        return value[:, :rows], value[:, rows, 0]

    def shifted(value, step):
        return lax.ppermute(value, axis, [(i, i + step) for i in range(count - step)])

    state, decay = split(shifted(packed, 1))
    decay = jnp.where(mine == 0, jnp.ones_like(decay), decay)
    step = 1
    if count > 2:
        older_state, older_decay = split(shifted(packed, 2))
        has = mine >= 2
        state = jnp.where(has, decay[:, None, None] * older_state + state, state)
        decay = jnp.where(has, older_decay * decay, decay)
        step = 2
    while step < count - 1:
        got_state, got_decay = split(shifted(jnp.concatenate([state, jnp.broadcast_to(decay[:, None, None], decay_row.shape)], axis=1), step))
        has = mine >= step
        state = jnp.where(has, decay[:, None, None] * got_state + state, state)
        decay = jnp.where(has, got_decay * decay, decay)
        step *= 2
    return state


def combine_state(earlier, later):
    return (earlier[0] * later[0], later[0][:, None, None] * earlier[1] + later[1])


def apply_experts(arrived, gate_weight, up_weight, down_weight):
    exp_dev = gate_weight.shape[0]
    item_count = arrived.shape[1]
    features = arrived.shape[2]
    grouped = arrived.reshape(-1, exp_dev, item_count, features)
    gate_act = jnp.einsum(
        "send,edf->senf", grouped, gate_weight, preferred_element_type=jnp.float32
    )
    up_act = jnp.einsum("send,edf->senf", grouped, up_weight, preferred_element_type=jnp.float32)
    inner_act = (jax.nn.silu(gate_act) * up_act).astype(jnp.bfloat16)
    result = jnp.einsum(
        "senf,efd->send", inner_act, down_weight, preferred_element_type=jnp.float32
    )
    return result.astype(jnp.bfloat16).reshape(-1, item_count, features)


def on_device(
    queries,
    keys,
    values,
    log_decay,
    resid,
    gate_in,
    attn_gain,
    moe_gain,
    router_weight,
    expert_ids,
    gate_weight,
    up_weight,
    down_weight,
):
    tok_rows = queries.shape[1]
    features = queries.shape[2]
    head_count = log_decay.shape[0]
    head_size = features // head_count
    inv_root = head_size ** (-0.5)
    q_rows = queries.reshape(tok_rows, head_count, head_size)
    k_rows = keys.reshape(tok_rows, head_count, head_size)
    v_rows = values.reshape(tok_rows, head_count, head_size)
    decay_log = log_decay.reshape(head_count, tok_rows)
    cumulated = jnp.cumsum(decay_log, axis=1)
    positions = jnp.arange(tok_rows, dtype=jnp.int32)
    causal = (positions[:, None] >= positions[None, :])[None]
    gap_log = jnp.where(causal, cumulated[:, :, None] - cumulated[:, None, :], 0.0)
    damping = jnp.where(causal, jnp.exp(gap_log), 0.0)
    scores = (
        jnp.einsum("thd,shd->hts", q_rows, k_rows, preferred_element_type=jnp.float32)
        * inv_root
        * damping
    )
    scores = scores.astype(jnp.bfloat16)
    local_part = jnp.einsum("hts,shd->thd", scores, v_rows, preferred_element_type=jnp.float32)
    block_decay = jnp.exp(cumulated[:, -1])
    tail_decay = jnp.exp(cumulated[:, -1:] - cumulated)
    k_scaled = k_rows.astype(jnp.float32) * tail_decay.T[:, :, None]
    contribution = jnp.einsum(
        "thd,the->hde", k_scaled, v_rows.astype(jnp.float32), precision=HIGHEST
    )
    entering = entering_scan(block_decay, contribution, "ctx")
    carried = (
        jnp.einsum("thd,hde->the", q_rows.astype(jnp.float32), entering, precision=HIGHEST)
        * (inv_root * jnp.exp(cumulated)).T[:, :, None]
    )
    attention = local_part + carried
    mean_square = jnp.mean(attention * attention, axis=-1, keepdims=True)
    flat_resid = resid.reshape(tok_rows, features)
    normalized = (attention * lax.rsqrt(mean_square + 1e-05)).reshape(
        tok_rows, features
    ) * attn_gain
    flat_rows = (
        flat_resid.astype(jnp.float32)
        + normalized * jax.nn.sigmoid(gate_in.reshape(tok_rows, features).astype(jnp.float32))
    ).astype(jnp.bfloat16)
    h_float = flat_rows.astype(jnp.float32)
    moe_square = jnp.mean(h_float * h_float, axis=-1, keepdims=True)
    normed = (h_float * lax.rsqrt(moe_square + 1e-06) * moe_gain).astype(jnp.bfloat16)
    top_count = expert_ids.shape[2]
    chosen = expert_ids.reshape(tok_rows, top_count)
    experts = gate_weight.shape[0] * lax.axis_size("exp")
    capacity = 2 * top_count * tok_rows // experts
    affinity = jax.nn.sigmoid(jnp.dot(normed, router_weight, preferred_element_type=jnp.float32))
    labels = jnp.arange(experts, dtype=jnp.int32)
    picks = (chosen[:, :, None] == labels[None, None, :]).astype(jnp.float32)
    picked = jnp.sum(picks * affinity[:, None, :], axis=2)
    shares = picked / jnp.sum(picked, axis=1, keepdims=True)
    listed = chosen.reshape(-1)
    onehot = (listed[:, None] == labels[None, :]).astype(jnp.int32)
    before = jnp.cumsum(onehot, axis=0) - onehot
    slot_index = listed * capacity + jnp.sum(before * onehot, axis=1)
    slot_labels = jnp.arange(experts * capacity, dtype=jnp.int32)
    placing = jnp.sum(
        slot_labels[:, None, None] == slot_index.reshape(tok_rows, top_count)[None], axis=2
    ).astype(jnp.bfloat16)
    outgoing = (
        jnp.dot(placing, normed, preferred_element_type=jnp.float32)
        .astype(jnp.bfloat16)
        .reshape(experts, capacity, features)
    )
    arrived = lax.all_to_all(outgoing, "exp", split_axis=0, concat_axis=0, tiled=True)
    produced = apply_experts(arrived, gate_weight, up_weight, down_weight)
    returned = lax.all_to_all(produced, "exp", split_axis=0, concat_axis=0, tiled=True)
    gathered = jnp.take(returned.reshape(-1, features), slot_index, axis=0).reshape(
        tok_rows, top_count, features
    )
    mixture = jnp.sum(shares[:, :, None] * gathered.astype(jnp.float32), axis=1)
    return (h_float + mixture).astype(jnp.bfloat16).reshape(1, tok_rows, features)


def solution(mesh):
    placed = (
        P("exp", "ctx", None),
        P("exp", "ctx", None),
        P("exp", "ctx", None),
        P(None, "exp", "ctx"),
        P("exp", "ctx", None),
        P("exp", "ctx", None),
        P(),
        P(),
        P(),
        P("exp", "ctx", None),
        P("exp", None, None),
        P("exp", None, None),
        P("exp", None, None),
    )
    return jax.shard_map(
        on_device, mesh=mesh, in_specs=placed, out_specs=P("exp", "ctx", None), check_vma=False
    )
```

```python
import jax
import jax.numpy as jnp
from jax import lax
from jax.sharding import PartitionSpec as P

HIGHEST = lax.Precision.HIGHEST


def entering_grid(block_decay, contribution, axis):
    count, mine = (lax.axis_size(axis), lax.axis_index(axis))
    width = int(round(count ** 0.5))
    if width * width != count or width < 2:
        return entering_scan(block_decay, contribution, axis)
    rows = contribution.shape[1]
    row_of, col_of = mine // width, mine % width

    def pack(state, decay):
        decay_row = jnp.broadcast_to(decay[:, None, None], state.shape[:1] + (1,) + state.shape[2:])
        return jnp.concatenate([state, decay_row], axis=1)

    def split(value):
        return value[:, :rows], value[:, rows, 0]

    def along_row(value, step):
        pairs = [(i, (i // width) * width + (i % width + step) % width) for i in range(count)]
        return split(lax.ppermute(value, axis, pairs))

    def along_col(value, step):
        pairs = [(i, ((i // width + step) % width) * width + i % width) for i in range(count)]
        return split(lax.ppermute(value, axis, pairs))

    def prefix(own_index, got):
        state = jnp.zeros_like(got[0][0])
        weight = jnp.ones_like(got[0][1])
        for step, (got_state, got_decay) in enumerate(got, start=1):
            has = own_index >= step
            state = jnp.where(has, weight[:, None, None] * got_state + state, state)
            weight = jnp.where(has, weight * got_decay, weight)
        return state, weight

    packed = pack(contribution, block_decay)
    in_row = [along_row(packed, step) for step in range(1, width)]
    before, before_decay = prefix(col_of, in_row)
    total = block_decay[:, None, None] * before + contribution
    total_decay = before_decay * block_decay
    for ahead in range(1, width):
        got_state, got_decay = in_row[width - 1 - ahead]
        has = col_of + ahead <= width - 1
        total = jnp.where(has, got_decay[:, None, None] * total + got_state, total)
        total_decay = jnp.where(has, total_decay * got_decay, total_decay)
    in_col = [along_col(pack(total, total_decay), step) for step in range(1, width)]
    entering_row, _ = prefix(row_of, in_col)
    return before_decay[:, None, None] * entering_row + before


def entering_scan(block_decay, contribution, axis):
    count, mine = (lax.axis_size(axis), lax.axis_index(axis))
    rows = contribution.shape[1]
    decay_row = jnp.broadcast_to(block_decay[:, None, None], contribution.shape[:1] + (1,) + contribution.shape[2:])
    packed = jnp.concatenate([contribution, decay_row], axis=1)

    def split(value):
        return value[:, :rows], value[:, rows, 0]

    def shifted(value, step):
        return lax.ppermute(value, axis, [(i, i + step) for i in range(count - step)])

    state, decay = split(shifted(packed, 1))
    decay = jnp.where(mine == 0, jnp.ones_like(decay), decay)
    step = 1
    if count > 2:
        older_state, older_decay = split(shifted(packed, 2))
        has = mine >= 2
        state = jnp.where(has, decay[:, None, None] * older_state + state, state)
        decay = jnp.where(has, older_decay * decay, decay)
        step = 2
    while step < count - 1:
        got_state, got_decay = split(shifted(jnp.concatenate([state, jnp.broadcast_to(decay[:, None, None], decay_row.shape)], axis=1), step))
        has = mine >= step
        state = jnp.where(has, decay[:, None, None] * got_state + state, state)
        decay = jnp.where(has, got_decay * decay, decay)
        step *= 2
    return state


def combine_state(earlier, later):
    return (earlier[0] * later[0], later[0][:, None, None] * earlier[1] + later[1])


def apply_experts(arrived, gate_weight, up_weight, down_weight):
    exp_dev = gate_weight.shape[0]
    item_count = arrived.shape[1]
    features = arrived.shape[2]
    grouped = arrived.reshape(-1, exp_dev, item_count, features)
    gate_act = jnp.einsum(
        "send,edf->senf", grouped, gate_weight, preferred_element_type=jnp.float32
    )
    up_act = jnp.einsum("send,edf->senf", grouped, up_weight, preferred_element_type=jnp.float32)
    inner_act = (jax.nn.silu(gate_act) * up_act).astype(jnp.bfloat16)
    result = jnp.einsum(
        "senf,efd->send", inner_act, down_weight, preferred_element_type=jnp.float32
    )
    return result.astype(jnp.bfloat16).reshape(-1, item_count, features)


def on_device(
    queries,
    keys,
    values,
    log_decay,
    resid,
    gate_in,
    attn_gain,
    moe_gain,
    router_weight,
    expert_ids,
    gate_weight,
    up_weight,
    down_weight,
):
    tok_rows = queries.shape[1]
    features = queries.shape[2]
    head_count = log_decay.shape[0]
    head_size = features // head_count
    inv_root = head_size ** (-0.5)
    q_rows = queries.reshape(tok_rows, head_count, head_size)
    k_rows = keys.reshape(tok_rows, head_count, head_size)
    v_rows = values.reshape(tok_rows, head_count, head_size)
    decay_log = log_decay.reshape(head_count, tok_rows)
    cumulated = jnp.cumsum(decay_log, axis=1)
    positions = jnp.arange(tok_rows, dtype=jnp.int32)
    causal = (positions[:, None] >= positions[None, :])[None]
    gap_log = jnp.where(causal, cumulated[:, :, None] - cumulated[:, None, :], 0.0)
    damping = jnp.where(causal, jnp.exp(gap_log), 0.0)
    scores = (
        jnp.einsum("thd,shd->hts", q_rows, k_rows, preferred_element_type=jnp.float32)
        * inv_root
        * damping
    )
    scores = scores.astype(jnp.bfloat16)
    local_part = jnp.einsum("hts,shd->thd", scores, v_rows, preferred_element_type=jnp.float32)
    block_decay = jnp.exp(cumulated[:, -1])
    tail_decay = jnp.exp(cumulated[:, -1:] - cumulated)
    k_scaled = k_rows.astype(jnp.float32) * tail_decay.T[:, :, None]
    contribution = jnp.einsum(
        "thd,the->hde", k_scaled, v_rows.astype(jnp.float32), precision=HIGHEST
    )
    entering = entering_grid(block_decay, contribution, "ctx")
    carried = (
        jnp.einsum("thd,hde->the", q_rows.astype(jnp.float32), entering, precision=HIGHEST)
        * (inv_root * jnp.exp(cumulated)).T[:, :, None]
    )
    attention = local_part + carried
    mean_square = jnp.mean(attention * attention, axis=-1, keepdims=True)
    flat_resid = resid.reshape(tok_rows, features)
    normalized = (attention * lax.rsqrt(mean_square + 1e-05)).reshape(
        tok_rows, features
    ) * attn_gain
    flat_rows = (
        flat_resid.astype(jnp.float32)
        + normalized * jax.nn.sigmoid(gate_in.reshape(tok_rows, features).astype(jnp.float32))
    ).astype(jnp.bfloat16)
    h_float = flat_rows.astype(jnp.float32)
    moe_square = jnp.mean(h_float * h_float, axis=-1, keepdims=True)
    normed = (h_float * lax.rsqrt(moe_square + 1e-06) * moe_gain).astype(jnp.bfloat16)
    top_count = expert_ids.shape[2]
    chosen = expert_ids.reshape(tok_rows, top_count)
    experts = gate_weight.shape[0] * lax.axis_size("exp")
    capacity = 2 * top_count * tok_rows // experts
    affinity = jax.nn.sigmoid(jnp.dot(normed, router_weight, preferred_element_type=jnp.float32))
    labels = jnp.arange(experts, dtype=jnp.int32)
    picks = (chosen[:, :, None] == labels[None, None, :]).astype(jnp.float32)
    picked = jnp.sum(picks * affinity[:, None, :], axis=2)
    shares = picked / jnp.sum(picked, axis=1, keepdims=True)
    listed = chosen.reshape(-1)
    onehot = (listed[:, None] == labels[None, :]).astype(jnp.int32)
    before = jnp.cumsum(onehot, axis=0) - onehot
    slot_index = listed * capacity + jnp.sum(before * onehot, axis=1)
    slot_labels = jnp.arange(experts * capacity, dtype=jnp.int32)
    placing = jnp.sum(
        slot_labels[:, None, None] == slot_index.reshape(tok_rows, top_count)[None], axis=2
    ).astype(jnp.bfloat16)
    outgoing = (
        jnp.dot(placing, normed, preferred_element_type=jnp.float32)
        .astype(jnp.bfloat16)
        .reshape(experts, capacity, features)
    )
    arrived = lax.all_to_all(outgoing, "exp", split_axis=0, concat_axis=0, tiled=True)
    produced = apply_experts(arrived, gate_weight, up_weight, down_weight)
    returned = lax.all_to_all(produced, "exp", split_axis=0, concat_axis=0, tiled=True)
    gathered = jnp.take(returned.reshape(-1, features), slot_index, axis=0).reshape(
        tok_rows, top_count, features
    )
    mixture = jnp.sum(shares[:, :, None] * gathered.astype(jnp.float32), axis=1)
    return (h_float + mixture).astype(jnp.bfloat16).reshape(1, tok_rows, features)


def solution(mesh):
    placed = (
        P("exp", "ctx", None),
        P("exp", "ctx", None),
        P("exp", "ctx", None),
        P(None, "exp", "ctx"),
        P("exp", "ctx", None),
        P("exp", "ctx", None),
        P(),
        P(),
        P(),
        P("exp", "ctx", None),
        P("exp", None, None),
        P("exp", None, None),
        P("exp", None, None),
    )
    return jax.shard_map(
        on_device, mesh=mesh, in_specs=placed, out_specs=P("exp", "ctx", None), check_vma=False
    )
```

```python
import jax
import jax.numpy as jnp
from jax import lax
from jax.sharding import PartitionSpec as P

HIGHEST = lax.Precision.HIGHEST


def entering_grid(block_decay, contribution, axis):
    count, mine = (lax.axis_size(axis), lax.axis_index(axis))
    width = int(round(count ** 0.5))
    if width * width != count or width < 2:
        return entering_scan(block_decay, contribution, axis)
    rows = contribution.shape[1]
    row_of, col_of = mine // width, mine % width

    def pack(state, decay):
        high = decay.astype(jnp.bfloat16)
        low = (decay - high.astype(jnp.float32)).astype(jnp.bfloat16)
        shape = state.shape[:1] + (1,) + state.shape[2:]
        decay_rows = [jnp.broadcast_to(part[:, None, None], shape) for part in (high, low)]
        return jnp.concatenate([state.astype(jnp.bfloat16)] + decay_rows, axis=1)

    def split(value):
        decay = value[:, rows, 0].astype(jnp.float32) + value[:, rows + 1, 0].astype(jnp.float32)
        return value[:, :rows].astype(jnp.float32), decay

    def along_row(value, step):
        pairs = [(i, (i // width) * width + (i % width + step) % width) for i in range(count)]
        return split(lax.ppermute(value, axis, pairs))

    def along_col(value, step):
        pairs = [(i, ((i // width + step) % width) * width + i % width) for i in range(count)]
        return split(lax.ppermute(value, axis, pairs))

    def prefix(own_index, got):
        state = jnp.zeros_like(got[0][0])
        weight = jnp.ones_like(got[0][1])
        for step, (got_state, got_decay) in enumerate(got, start=1):
            has = own_index >= step
            state = jnp.where(has, weight[:, None, None] * got_state + state, state)
            weight = jnp.where(has, weight * got_decay, weight)
        return state, weight

    packed = pack(contribution, block_decay)
    in_row = [along_row(packed, step) for step in range(1, width)]
    before, before_decay = prefix(col_of, in_row)
    total = block_decay[:, None, None] * before + contribution
    total_decay = before_decay * block_decay
    for ahead in range(1, width):
        got_state, got_decay = in_row[width - 1 - ahead]
        has = col_of + ahead <= width - 1
        total = jnp.where(has, got_decay[:, None, None] * total + got_state, total)
        total_decay = jnp.where(has, total_decay * got_decay, total_decay)
    in_col = [along_col(pack(total, total_decay), step) for step in range(1, width)]
    entering_row, _ = prefix(row_of, in_col)
    return before_decay[:, None, None] * entering_row + before


def entering_scan(block_decay, contribution, axis):
    count, mine = (lax.axis_size(axis), lax.axis_index(axis))
    rows = contribution.shape[1]
    decay_row = jnp.broadcast_to(block_decay[:, None, None], contribution.shape[:1] + (1,) + contribution.shape[2:])
    packed = jnp.concatenate([contribution, decay_row], axis=1)

    def split(value):
        return value[:, :rows], value[:, rows, 0]

    def shifted(value, step):
        return lax.ppermute(value, axis, [(i, i + step) for i in range(count - step)])

    state, decay = split(shifted(packed, 1))
    decay = jnp.where(mine == 0, jnp.ones_like(decay), decay)
    step = 1
    if count > 2:
        older_state, older_decay = split(shifted(packed, 2))
        has = mine >= 2
        state = jnp.where(has, decay[:, None, None] * older_state + state, state)
        decay = jnp.where(has, older_decay * decay, decay)
        step = 2
    while step < count - 1:
        got_state, got_decay = split(shifted(jnp.concatenate([state, jnp.broadcast_to(decay[:, None, None], decay_row.shape)], axis=1), step))
        has = mine >= step
        state = jnp.where(has, decay[:, None, None] * got_state + state, state)
        decay = jnp.where(has, got_decay * decay, decay)
        step *= 2
    return state


def combine_state(earlier, later):
    return (earlier[0] * later[0], later[0][:, None, None] * earlier[1] + later[1])


def apply_experts(arrived, gate_weight, up_weight, down_weight):
    exp_dev = gate_weight.shape[0]
    item_count = arrived.shape[1]
    features = arrived.shape[2]
    grouped = arrived.reshape(-1, exp_dev, item_count, features)
    gate_act = jnp.einsum(
        "send,edf->senf", grouped, gate_weight, preferred_element_type=jnp.float32
    )
    up_act = jnp.einsum("send,edf->senf", grouped, up_weight, preferred_element_type=jnp.float32)
    inner_act = (jax.nn.silu(gate_act) * up_act).astype(jnp.bfloat16)
    result = jnp.einsum(
        "senf,efd->send", inner_act, down_weight, preferred_element_type=jnp.float32
    )
    return result.astype(jnp.bfloat16).reshape(-1, item_count, features)


def on_device(
    queries,
    keys,
    values,
    log_decay,
    resid,
    gate_in,
    attn_gain,
    moe_gain,
    router_weight,
    expert_ids,
    gate_weight,
    up_weight,
    down_weight,
):
    tok_rows = queries.shape[1]
    features = queries.shape[2]
    head_count = log_decay.shape[0]
    head_size = features // head_count
    inv_root = head_size ** (-0.5)
    q_rows = queries.reshape(tok_rows, head_count, head_size)
    k_rows = keys.reshape(tok_rows, head_count, head_size)
    v_rows = values.reshape(tok_rows, head_count, head_size)
    decay_log = log_decay.reshape(head_count, tok_rows)
    cumulated = jnp.cumsum(decay_log, axis=1)
    positions = jnp.arange(tok_rows, dtype=jnp.int32)
    causal = (positions[:, None] >= positions[None, :])[None]
    gap_log = jnp.where(causal, cumulated[:, :, None] - cumulated[:, None, :], 0.0)
    damping = jnp.where(causal, jnp.exp(gap_log), 0.0)
    scores = (
        jnp.einsum("thd,shd->hts", q_rows, k_rows, preferred_element_type=jnp.float32)
        * inv_root
        * damping
    )
    scores = scores.astype(jnp.bfloat16)
    local_part = jnp.einsum("hts,shd->thd", scores, v_rows, preferred_element_type=jnp.float32)
    block_decay = jnp.exp(cumulated[:, -1])
    tail_decay = jnp.exp(cumulated[:, -1:] - cumulated)
    k_scaled = k_rows.astype(jnp.float32) * tail_decay.T[:, :, None]
    contribution = jnp.einsum(
        "thd,the->hde", k_scaled, v_rows.astype(jnp.float32), precision=HIGHEST
    )
    entering = entering_grid(block_decay, contribution, "ctx")
    carried = (
        jnp.einsum("thd,hde->the", q_rows.astype(jnp.float32), entering, precision=HIGHEST)
        * (inv_root * jnp.exp(cumulated)).T[:, :, None]
    )
    attention = local_part + carried
    mean_square = jnp.mean(attention * attention, axis=-1, keepdims=True)
    flat_resid = resid.reshape(tok_rows, features)
    normalized = (attention * lax.rsqrt(mean_square + 1e-05)).reshape(
        tok_rows, features
    ) * attn_gain
    flat_rows = (
        flat_resid.astype(jnp.float32)
        + normalized * jax.nn.sigmoid(gate_in.reshape(tok_rows, features).astype(jnp.float32))
    ).astype(jnp.bfloat16)
    h_float = flat_rows.astype(jnp.float32)
    moe_square = jnp.mean(h_float * h_float, axis=-1, keepdims=True)
    normed = (h_float * lax.rsqrt(moe_square + 1e-06) * moe_gain).astype(jnp.bfloat16)
    top_count = expert_ids.shape[2]
    chosen = expert_ids.reshape(tok_rows, top_count)
    experts = gate_weight.shape[0] * lax.axis_size("exp")
    capacity = 2 * top_count * tok_rows // experts
    affinity = jax.nn.sigmoid(jnp.dot(normed, router_weight, preferred_element_type=jnp.float32))
    labels = jnp.arange(experts, dtype=jnp.int32)
    picks = (chosen[:, :, None] == labels[None, None, :]).astype(jnp.float32)
    picked = jnp.sum(picks * affinity[:, None, :], axis=2)
    shares = picked / jnp.sum(picked, axis=1, keepdims=True)
    listed = chosen.reshape(-1)
    onehot = (listed[:, None] == labels[None, :]).astype(jnp.int32)
    before = jnp.cumsum(onehot, axis=0) - onehot
    slot_index = listed * capacity + jnp.sum(before * onehot, axis=1)
    slot_labels = jnp.arange(experts * capacity, dtype=jnp.int32)
    placing = jnp.sum(
        slot_labels[:, None, None] == slot_index.reshape(tok_rows, top_count)[None], axis=2
    ).astype(jnp.bfloat16)
    outgoing = (
        jnp.dot(placing, normed, preferred_element_type=jnp.float32)
        .astype(jnp.bfloat16)
        .reshape(experts, capacity, features)
    )
    arrived = lax.all_to_all(outgoing, "exp", split_axis=0, concat_axis=0, tiled=True)
    produced = apply_experts(arrived, gate_weight, up_weight, down_weight)
    returned = lax.all_to_all(produced, "exp", split_axis=0, concat_axis=0, tiled=True)
    gathered = jnp.take(returned.reshape(-1, features), slot_index, axis=0).reshape(
        tok_rows, top_count, features
    )
    mixture = jnp.sum(shares[:, :, None] * gathered.astype(jnp.float32), axis=1)
    return (h_float + mixture).astype(jnp.bfloat16).reshape(1, tok_rows, features)


def solution(mesh):
    placed = (
        P("exp", "ctx", None),
        P("exp", "ctx", None),
        P("exp", "ctx", None),
        P(None, "exp", "ctx"),
        P("exp", "ctx", None),
        P("exp", "ctx", None),
        P(),
        P(),
        P(),
        P("exp", "ctx", None),
        P("exp", None, None),
        P("exp", None, None),
        P("exp", None, None),
    )
    return jax.shard_map(
        on_device, mesh=mesh, in_specs=placed, out_specs=P("exp", "ctx", None), check_vma=False
    )
```

```python
import jax
import jax.numpy as jnp
from jax import lax
from jax.sharding import PartitionSpec as P

HIGHEST = lax.Precision.HIGHEST


def entering_grid(block_decay, contribution, axis):
    count, mine = (lax.axis_size(axis), lax.axis_index(axis))
    width = int(round(count ** 0.5))
    if width * width != count or width < 2:
        return entering_scan(block_decay, contribution, axis)
    rows = contribution.shape[1]
    row_of, col_of = mine // width, mine % width

    def pack(state, decay):
        high = decay.astype(jnp.bfloat16)
        low = (decay - high.astype(jnp.float32)).astype(jnp.bfloat16)
        shape = state.shape[:1] + (1,) + state.shape[2:]
        decay_rows = [jnp.broadcast_to(part[:, None, None], shape) for part in (high, low)]
        return jnp.concatenate([state.astype(jnp.bfloat16)] + decay_rows, axis=1)

    def split(value):
        decay = value[:, rows, 0].astype(jnp.float32) + value[:, rows + 1, 0].astype(jnp.float32)
        return value[:, :rows].astype(jnp.float32), decay

    def along_row(value, step):
        pairs = [(i, (i // width) * width + (i % width + step) % width) for i in range(count)]
        return split(lax.ppermute(value, axis, pairs))

    def along_col(value, step):
        pairs = [(i, (i // width + step) * width + i % width) for i in range(count - step * width)]
        return split(lax.ppermute(value, axis, pairs))

    def prefix(own_index, got):
        state = jnp.zeros_like(got[0][0])
        weight = jnp.ones_like(got[0][1])
        for step, (got_state, got_decay) in enumerate(got, start=1):
            has = own_index >= step
            state = jnp.where(has, weight[:, None, None] * got_state + state, state)
            weight = jnp.where(has, weight * got_decay, weight)
        return state, weight

    packed = pack(contribution, block_decay)
    in_row = [along_row(packed, step) for step in range(1, width)]
    before, before_decay = prefix(col_of, in_row)
    total = block_decay[:, None, None] * before + contribution
    total_decay = before_decay * block_decay
    for ahead in range(1, width):
        got_state, got_decay = in_row[width - 1 - ahead]
        has = col_of + ahead <= width - 1
        total = jnp.where(has, got_decay[:, None, None] * total + got_state, total)
        total_decay = jnp.where(has, total_decay * got_decay, total_decay)
    in_col = [along_col(pack(total, total_decay), step) for step in range(1, width)]
    entering_row, _ = prefix(row_of, in_col)
    return before_decay[:, None, None] * entering_row + before


def entering_scan(block_decay, contribution, axis):
    count, mine = (lax.axis_size(axis), lax.axis_index(axis))
    rows = contribution.shape[1]
    decay_row = jnp.broadcast_to(block_decay[:, None, None], contribution.shape[:1] + (1,) + contribution.shape[2:])
    packed = jnp.concatenate([contribution, decay_row], axis=1)

    def split(value):
        return value[:, :rows], value[:, rows, 0]

    def shifted(value, step):
        return lax.ppermute(value, axis, [(i, i + step) for i in range(count - step)])

    state, decay = split(shifted(packed, 1))
    decay = jnp.where(mine == 0, jnp.ones_like(decay), decay)
    step = 1
    if count > 2:
        older_state, older_decay = split(shifted(packed, 2))
        has = mine >= 2
        state = jnp.where(has, decay[:, None, None] * older_state + state, state)
        decay = jnp.where(has, older_decay * decay, decay)
        step = 2
    while step < count - 1:
        got_state, got_decay = split(shifted(jnp.concatenate([state, jnp.broadcast_to(decay[:, None, None], decay_row.shape)], axis=1), step))
        has = mine >= step
        state = jnp.where(has, decay[:, None, None] * got_state + state, state)
        decay = jnp.where(has, got_decay * decay, decay)
        step *= 2
    return state


def combine_state(earlier, later):
    return (earlier[0] * later[0], later[0][:, None, None] * earlier[1] + later[1])


def apply_experts(arrived, gate_weight, up_weight, down_weight):
    exp_dev = gate_weight.shape[0]
    item_count = arrived.shape[1]
    features = arrived.shape[2]
    grouped = arrived.reshape(-1, exp_dev, item_count, features)
    gate_act = jnp.einsum(
        "send,edf->senf", grouped, gate_weight, preferred_element_type=jnp.float32
    )
    up_act = jnp.einsum("send,edf->senf", grouped, up_weight, preferred_element_type=jnp.float32)
    inner_act = (jax.nn.silu(gate_act) * up_act).astype(jnp.bfloat16)
    result = jnp.einsum(
        "senf,efd->send", inner_act, down_weight, preferred_element_type=jnp.float32
    )
    return result.astype(jnp.bfloat16).reshape(-1, item_count, features)


def on_device(
    queries,
    keys,
    values,
    log_decay,
    resid,
    gate_in,
    attn_gain,
    moe_gain,
    router_weight,
    expert_ids,
    gate_weight,
    up_weight,
    down_weight,
):
    tok_rows = queries.shape[1]
    features = queries.shape[2]
    head_count = log_decay.shape[0]
    head_size = features // head_count
    inv_root = head_size ** (-0.5)
    q_rows = queries.reshape(tok_rows, head_count, head_size)
    k_rows = keys.reshape(tok_rows, head_count, head_size)
    v_rows = values.reshape(tok_rows, head_count, head_size)
    decay_log = log_decay.reshape(head_count, tok_rows)
    cumulated = jnp.cumsum(decay_log, axis=1)
    positions = jnp.arange(tok_rows, dtype=jnp.int32)
    causal = (positions[:, None] >= positions[None, :])[None]
    gap_log = jnp.where(causal, cumulated[:, :, None] - cumulated[:, None, :], 0.0)
    damping = jnp.where(causal, jnp.exp(gap_log), 0.0)
    scores = (
        jnp.einsum("thd,shd->hts", q_rows, k_rows, preferred_element_type=jnp.float32)
        * inv_root
        * damping
    )
    scores = scores.astype(jnp.bfloat16)
    local_part = jnp.einsum("hts,shd->thd", scores, v_rows, preferred_element_type=jnp.float32)
    block_decay = jnp.exp(cumulated[:, -1])
    tail_decay = jnp.exp(cumulated[:, -1:] - cumulated)
    k_scaled = k_rows.astype(jnp.float32) * tail_decay.T[:, :, None]
    contribution = jnp.einsum(
        "thd,the->hde", k_scaled, v_rows.astype(jnp.float32), precision=HIGHEST
    )
    entering = entering_grid(block_decay, contribution, "ctx")
    carried = (
        jnp.einsum("thd,hde->the", q_rows.astype(jnp.float32), entering, precision=HIGHEST)
        * (inv_root * jnp.exp(cumulated)).T[:, :, None]
    )
    attention = local_part + carried
    mean_square = jnp.mean(attention * attention, axis=-1, keepdims=True)
    flat_resid = resid.reshape(tok_rows, features)
    normalized = (attention * lax.rsqrt(mean_square + 1e-05)).reshape(
        tok_rows, features
    ) * attn_gain
    flat_rows = (
        flat_resid.astype(jnp.float32)
        + normalized * jax.nn.sigmoid(gate_in.reshape(tok_rows, features).astype(jnp.float32))
    ).astype(jnp.bfloat16)
    h_float = flat_rows.astype(jnp.float32)
    moe_square = jnp.mean(h_float * h_float, axis=-1, keepdims=True)
    normed = (h_float * lax.rsqrt(moe_square + 1e-06) * moe_gain).astype(jnp.bfloat16)
    top_count = expert_ids.shape[2]
    chosen = expert_ids.reshape(tok_rows, top_count)
    experts = gate_weight.shape[0] * lax.axis_size("exp")
    capacity = 2 * top_count * tok_rows // experts
    affinity = jax.nn.sigmoid(jnp.dot(normed, router_weight, preferred_element_type=jnp.float32))
    labels = jnp.arange(experts, dtype=jnp.int32)
    picks = (chosen[:, :, None] == labels[None, None, :]).astype(jnp.float32)
    picked = jnp.sum(picks * affinity[:, None, :], axis=2)
    shares = picked / jnp.sum(picked, axis=1, keepdims=True)
    listed = chosen.reshape(-1)
    onehot = (listed[:, None] == labels[None, :]).astype(jnp.int32)
    before = jnp.cumsum(onehot, axis=0) - onehot
    slot_index = listed * capacity + jnp.sum(before * onehot, axis=1)
    slot_labels = jnp.arange(experts * capacity, dtype=jnp.int32)
    placing = jnp.sum(
        slot_labels[:, None, None] == slot_index.reshape(tok_rows, top_count)[None], axis=2
    ).astype(jnp.bfloat16)
    outgoing = (
        jnp.dot(placing, normed, preferred_element_type=jnp.float32)
        .astype(jnp.bfloat16)
        .reshape(experts, capacity, features)
    )
    arrived = lax.all_to_all(outgoing, "exp", split_axis=0, concat_axis=0, tiled=True)
    produced = apply_experts(arrived, gate_weight, up_weight, down_weight)
    returned = lax.all_to_all(produced, "exp", split_axis=0, concat_axis=0, tiled=True)
    gathered = jnp.take(returned.reshape(-1, features), slot_index, axis=0).reshape(
        tok_rows, top_count, features
    )
    mixture = jnp.sum(shares[:, :, None] * gathered.astype(jnp.float32), axis=1)
    return (h_float + mixture).astype(jnp.bfloat16).reshape(1, tok_rows, features)


def solution(mesh):
    placed = (
        P("exp", "ctx", None),
        P("exp", "ctx", None),
        P("exp", "ctx", None),
        P(None, "exp", "ctx"),
        P("exp", "ctx", None),
        P("exp", "ctx", None),
        P(),
        P(),
        P(),
        P("exp", "ctx", None),
        P("exp", None, None),
        P("exp", None, None),
        P("exp", None, None),
    )
    return jax.shard_map(
        on_device, mesh=mesh, in_specs=placed, out_specs=P("exp", "ctx", None), check_vma=False
    )
```

```python
import jax
import jax.numpy as jnp
from jax import lax
from jax.sharding import PartitionSpec as P

HIGHEST = lax.Precision.HIGHEST


def entering_grid(block_decay, contribution, axis):
    count, mine = (lax.axis_size(axis), lax.axis_index(axis))
    width = int(round(count ** 0.5))
    if width * width != count or width < 2:
        return entering_scan(block_decay, contribution, axis)
    rows = contribution.shape[1]
    row_of, col_of = mine // width, mine % width

    def pack(state, decay):
        high = decay.astype(jnp.bfloat16)
        low = (decay - high.astype(jnp.float32)).astype(jnp.bfloat16)
        shape = state.shape[:1] + (1,) + state.shape[2:]
        decay_rows = [jnp.broadcast_to(part[:, None, None], shape) for part in (high, low)]
        return jnp.concatenate([state.astype(jnp.bfloat16)] + decay_rows, axis=1)

    def split(value):
        decay = value[:, rows, 0].astype(jnp.float32) + value[:, rows + 1, 0].astype(jnp.float32)
        return value[:, :rows].astype(jnp.float32), decay

    def along_row(value, step):
        pairs = [(i, (i // width) * width + (i % width + step) % width) for i in range(count)]
        return split(lax.ppermute(value, axis, pairs))

    def along_col(value, step):
        pairs = [(i, ((i // width + step) % width) * width + i % width) for i in range(count)]
        return split(lax.ppermute(value, axis, pairs))

    def prefix(own_index, got):
        state = jnp.zeros_like(got[0][0])
        weight = jnp.ones_like(got[0][1])
        for step, (got_state, got_decay) in enumerate(got, start=1):
            has = own_index >= step
            state = jnp.where(has, weight[:, None, None] * got_state + state, state)
            weight = jnp.where(has, weight * got_decay, weight)
        return state, weight

    packed = pack(contribution, block_decay)
    in_row = [along_row(packed, step) for step in range(1, width)]
    before, before_decay = prefix(col_of, in_row)
    total = block_decay[:, None, None] * before + contribution
    total_decay = before_decay * block_decay
    for ahead in range(1, width):
        got_state, got_decay = in_row[width - 1 - ahead]
        has = col_of + ahead <= width - 1
        total = jnp.where(has, got_decay[:, None, None] * total + got_state, total)
        total_decay = jnp.where(has, total_decay * got_decay, total_decay)
    in_col = [along_col(pack(total, total_decay), step) for step in range(1, width)]
    entering_row, _ = prefix(row_of, in_col)
    return before_decay[:, None, None] * entering_row + before


def entering_scan(block_decay, contribution, axis):
    count, mine = (lax.axis_size(axis), lax.axis_index(axis))
    rows = contribution.shape[1]
    decay_row = jnp.broadcast_to(block_decay[:, None, None], contribution.shape[:1] + (1,) + contribution.shape[2:])
    packed = jnp.concatenate([contribution, decay_row], axis=1)

    def split(value):
        return value[:, :rows], value[:, rows, 0]

    def shifted(value, step):
        return lax.ppermute(value, axis, [(i, i + step) for i in range(count - step)])

    state, decay = split(shifted(packed, 1))
    decay = jnp.where(mine == 0, jnp.ones_like(decay), decay)
    step = 1
    if count > 2:
        older_state, older_decay = split(shifted(packed, 2))
        has = mine >= 2
        state = jnp.where(has, decay[:, None, None] * older_state + state, state)
        decay = jnp.where(has, older_decay * decay, decay)
        step = 2
    while step < count - 1:
        got_state, got_decay = split(shifted(jnp.concatenate([state, jnp.broadcast_to(decay[:, None, None], decay_row.shape)], axis=1), step))
        has = mine >= step
        state = jnp.where(has, decay[:, None, None] * got_state + state, state)
        decay = jnp.where(has, got_decay * decay, decay)
        step *= 2
    return state


def combine_state(earlier, later):
    return (earlier[0] * later[0], later[0][:, None, None] * earlier[1] + later[1])


def apply_experts(arrived, gate_weight, up_weight, down_weight):
    exp_dev = gate_weight.shape[0]
    item_count = arrived.shape[1]
    features = arrived.shape[2]
    grouped = arrived.reshape(-1, exp_dev, item_count, features)
    gate_act = jnp.einsum(
        "send,edf->senf", grouped, gate_weight, preferred_element_type=jnp.float32
    )
    up_act = jnp.einsum("send,edf->senf", grouped, up_weight, preferred_element_type=jnp.float32)
    inner_act = (jax.nn.silu(gate_act) * up_act).astype(jnp.bfloat16)
    result = jnp.einsum(
        "senf,efd->send", inner_act, down_weight, preferred_element_type=jnp.float32
    )
    return result.astype(jnp.bfloat16).reshape(-1, item_count, features)


def on_device(
    queries,
    keys,
    values,
    log_decay,
    resid,
    gate_in,
    attn_gain,
    moe_gain,
    router_weight,
    expert_ids,
    gate_weight,
    up_weight,
    down_weight,
):
    tok_rows = queries.shape[1]
    features = queries.shape[2]
    head_count = log_decay.shape[0]
    head_size = features // head_count
    inv_root = head_size ** (-0.5)
    q_rows = queries.reshape(tok_rows, head_count, head_size)
    k_rows = keys.reshape(tok_rows, head_count, head_size)
    v_rows = values.reshape(tok_rows, head_count, head_size)
    decay_log = log_decay.reshape(head_count, tok_rows)
    cumulated = jnp.cumsum(decay_log, axis=1)
    positions = jnp.arange(tok_rows, dtype=jnp.int32)
    causal = (positions[:, None] >= positions[None, :])[None]
    gap_log = jnp.where(causal, cumulated[:, :, None] - cumulated[:, None, :], 0.0)
    damping = jnp.where(causal, jnp.exp(gap_log), 0.0)
    scores = (
        jnp.einsum("thd,shd->hts", q_rows, k_rows, preferred_element_type=jnp.float32)
        * inv_root
        * damping
    )
    scores = scores.astype(jnp.bfloat16)
    local_part = jnp.einsum("hts,shd->thd", scores, v_rows, preferred_element_type=jnp.float32)
    block_decay = jnp.exp(cumulated[:, -1])
    tail_decay = jnp.exp(cumulated[:, -1:] - cumulated)
    k_scaled = k_rows.astype(jnp.float32) * tail_decay.T[:, :, None]
    contribution = jnp.einsum(
        "thd,the->hde", k_scaled, v_rows.astype(jnp.float32), precision=HIGHEST
    )
    entering = entering_grid(block_decay, contribution, "ctx")
    carried = (
        jnp.einsum("thd,hde->the", q_rows.astype(jnp.float32), entering, precision=HIGHEST)
        * (inv_root * jnp.exp(cumulated)).T[:, :, None]
    )
    attention = local_part + carried
    mean_square = jnp.mean(attention * attention, axis=-1, keepdims=True)
    flat_resid = resid.reshape(tok_rows, features)
    normalized = (attention * lax.rsqrt(mean_square + 1e-05)).reshape(
        tok_rows, features
    ) * attn_gain
    flat_rows = (
        flat_resid.astype(jnp.float32)
        + normalized * jax.nn.sigmoid(gate_in.reshape(tok_rows, features).astype(jnp.float32))
    ).astype(jnp.bfloat16)
    h_float = flat_rows.astype(jnp.float32)
    moe_square = jnp.mean(h_float * h_float, axis=-1, keepdims=True)
    normed = (h_float * lax.rsqrt(moe_square + 1e-06) * moe_gain).astype(jnp.bfloat16)
    top_count = expert_ids.shape[2]
    chosen = expert_ids.reshape(tok_rows, top_count)
    experts = gate_weight.shape[0] * lax.axis_size("exp")
    capacity = 2 * top_count * tok_rows // experts
    affinity = jax.nn.sigmoid(jnp.dot(normed, router_weight, preferred_element_type=jnp.float32))
    labels = jnp.arange(experts, dtype=jnp.int32)
    picks = (chosen[:, :, None] == labels[None, None, :]).astype(jnp.float32)
    picked = jnp.sum(picks * affinity[:, None, :], axis=2)
    shares = picked / jnp.sum(picked, axis=1, keepdims=True)
    listed = chosen.reshape(-1)
    onehot = (listed[:, None] == labels[None, :]).astype(jnp.int32)
    before = jnp.cumsum(onehot, axis=0) - onehot
    slot_index = listed * capacity + jnp.sum(before * onehot, axis=1)
    slot_labels = jnp.arange(experts * capacity, dtype=jnp.int32)
    placing = jnp.sum(
        slot_labels[:, None, None] == slot_index.reshape(tok_rows, top_count)[None], axis=2
    ).astype(jnp.bfloat16)
    outgoing = (
        jnp.dot(placing, normed, preferred_element_type=jnp.float32)
        .astype(jnp.bfloat16)
        .reshape(experts, capacity, features)
    )
    arrived = lax.all_to_all(outgoing, "exp", split_axis=0, concat_axis=0, tiled=True)
    produced = apply_experts(arrived, gate_weight, up_weight, down_weight)
    returned = lax.all_to_all(produced, "exp", split_axis=0, concat_axis=0, tiled=True)
    returned_rows = returned.reshape(-1, features)
    slot_pairs = slot_index.reshape(tok_rows, top_count)
    mixture = jnp.zeros((tok_rows, features), jnp.float32)
    for choice in range(top_count):
        picking = (slot_pairs[:, choice, None] == slot_labels[None, :]).astype(jnp.bfloat16)
        gathered = jnp.dot(picking, returned_rows, preferred_element_type=jnp.float32)
        mixture = mixture + shares[:, choice, None] * gathered
    return (h_float + mixture).astype(jnp.bfloat16).reshape(1, tok_rows, features)


def solution(mesh):
    placed = (
        P("exp", "ctx", None),
        P("exp", "ctx", None),
        P("exp", "ctx", None),
        P(None, "exp", "ctx"),
        P("exp", "ctx", None),
        P("exp", "ctx", None),
        P(),
        P(),
        P(),
        P("exp", "ctx", None),
        P("exp", None, None),
        P("exp", None, None),
        P("exp", None, None),
    )
    return jax.shard_map(
        on_device, mesh=mesh, in_specs=placed, out_specs=P("exp", "ctx", None), check_vma=False
    )
```
